32 devices in a mesh: row: 4 (over x, core), col: 8 (over z, y).
Axes of the slice: x: 2, y: 2, z: 4, core: 2. Of those that a mesh axis runs over, the one named last changes fastest.
Arguments:
- tiles: bfloat16 [160, 1024, 1024], P(('row', 'col')), may hold values from 5 to 500
- tile_list: int32 [160], P(('row', 'col')), may hold values from 0 to 7, as said below
- tile_count: int32 [32], P(('row', 'col')), may hold values from 1 to 5, as said below
- w_rows: float32 [8192, 256], P(('row', 'col')), may hold values from 0.01 to 3, as said below
- h_cols: float32 [256, 32768], P(None, ('row', 'col')), may hold values from 0.05 to 1
Outputs:
- h_next: float32 [256, 32768], P(None, ('row', 'col'))
The draws below stay inside these ranges and needn't reach their ends.
Inputs may be any that keep to these rules, and one draw needn't show every extreme that they name: `tile_list`: within the first tile_count[b] slots of column block b the row blocks are distinct; slots past the count hold row blocks that are ignored. `tile_count`: some column block has all 5 slots live in every draw. `w_rows`: entries are positive.
All inputs are finite; a program needn't handle non-finite values.
Results may differ from the reference program's by a relative error of at most 0.0003.
Values may be sent and summed in bfloat16 or wider, within the bound.
No kernel may reach another device: no remote copies, remote signals or barrier semaphores. Data moves between devices by JAX's collectives and lax.ppermute only.
A program may use at most 64 MiB of HBM per device.

```python
import math
import jax
import jax.numpy as jnp
from jax import lax

RANK = 256
TILE = 1024
SLOTS = 5
ROW_BLOCKS = 8
ROWS = 8192
SLOT_TOTAL = 160
COLS = 32768
DEVICES = 32


def tile_plan(key):
    plan_key = jax.random.fold_in(key, 7)
    subkeys = jax.random.split(plan_key, DEVICES + 3)

    def device_slots(device_key):
        return jax.random.permutation(device_key, ROW_BLOCKS)[:SLOTS]
    chosen = jax.vmap(device_slots)(subkeys[:DEVICES])
    light_count = jax.random.randint(subkeys[DEVICES], (DEVICES,), 1, 3)
    heavy_device = jax.random.randint(subkeys[DEVICES + 1], (DEVICES,), 0, 8) == 0
    counts = jnp.where(heavy_device, SLOTS, light_count)
    forced = jax.random.randint(subkeys[DEVICES + 2], (), 0, DEVICES)
    counts = jnp.where(jnp.arange(DEVICES, dtype=jnp.int32) == forced, SLOTS, counts)
    return (chosen.reshape(DEVICES * SLOTS).astype(jnp.int32), counts.astype(jnp.int32))


def draw_tile_list(key, part):
    return tile_plan(key)[0]


def draw_tile_count(key, part):
    return tile_plan(key)[1]


def draw_w_rows(key, part):
    position = jnp.arange(ROWS, dtype=jnp.float32)[:, None]
    slope = 1.0 + 2.0 * position / ROWS
    logs = jax.random.uniform(key, (ROWS, RANK), jnp.float32, math.log(0.01), 0.0)
    values = jnp.exp(logs)
    return values * slope


def steps_of(stream_key, extent, cuts, smallest, top_value):
    def one(dim, shards_of):
        draws = jax.random.uniform(jax.random.fold_in(jax.random.fold_in(stream_key, 6), dim), (shards_of,), jnp.float32, smallest / len(cuts), top_value / len(cuts))
        return jnp.repeat(jnp.exp(draws), extent[dim] // shards_of).reshape((-1,) + (1,) * (len(extent) - dim - 1))

    gain = one(*cuts[0])
    for cut in cuts[1:]:
        gain = gain * one(*cut)
    return gain


def setup_inputs(seed: int = 0) -> dict:
    keys = jax.random.split(jax.random.key(seed), 6)
    return {
        "tiles": jnp.clip(jnp.exp(math.log(500.0) - 4.6051702 * jax.random.uniform(keys[0], (SLOT_TOTAL, TILE, TILE), jnp.float32) ** steps_of(keys[0], (SLOT_TOTAL, TILE, TILE), ((0, 32),), -0.2, 0.2)), 5.0, 500.0).astype(jnp.bfloat16),
        "tile_list": draw_tile_list(jax.random.fold_in(keys[5], 71), 0),
        "tile_count": draw_tile_count(jax.random.fold_in(keys[5], 71), 0),
        "w_rows": draw_w_rows(jax.random.fold_in(keys[5], 71), 0),
        "h_cols": jnp.clip(jnp.exp(math.log(1.0) - 2.9957323 * jax.random.uniform(keys[4], (RANK, COLS), jnp.float32) ** steps_of(keys[4], (RANK, COLS), ((1, 32),), -0.2, 0.2)), 0.05, 1.0),
    }


def reference(tiles, tile_list, tile_count, w_rows, h_cols):
    w_half = w_rows.astype(jnp.bfloat16)
    gram_matrix = jnp.dot(w_half.T, w_half, preferred_element_type=jnp.float32)
    slot_ids = jnp.arange(SLOT_TOTAL, dtype=jnp.int32)
    owners = slot_ids // SLOTS
    is_live = (slot_ids % SLOTS) < tile_count[owners]

    def add_tile(numerator, element):
        square, row_block, owner_id, active = element

        def add_block(total_now):
            w_block = lax.dynamic_slice_in_dim(w_half, (row_block * TILE).astype(jnp.int32), TILE, 0)
            product = lax.dot_general(w_block, square, (((0,), (0,)), ((), ())), preferred_element_type=jnp.float32)
            offset = (owner_id * TILE).astype(jnp.int32)
            before = lax.dynamic_slice_in_dim(total_now, offset, TILE, 1)
            return lax.dynamic_update_slice_in_dim(total_now, before + product, offset, 1)

        return lax.cond(active, add_block, lambda total_now: total_now, numerator), None

    numerator, _ = lax.scan(add_tile, jnp.zeros((RANK, COLS), jnp.float32), (tiles, tile_list, owners, is_live))
    denominator = jnp.dot(gram_matrix, h_cols, precision=lax.Precision.HIGHEST, preferred_element_type=jnp.float32)
    return h_cols * numerator / denominator
```

```python
import jax
import jax.numpy as jnp
from jax import lax
from jax.sharding import PartitionSpec as P

contract_rows = (((0,), (0,)), ((), ()))


def shards(tiles, tile_list, tile_count, w_rows, h_cols):
    slots, tile = tiles.shape[0], tiles.shape[1]
    rank_size = h_cols.shape[0]
    w_half = w_rows.astype(jnp.bfloat16)
    w_full = lax.all_gather(w_half, ("row", "col"), axis=0, tiled=True)
    gram = lax.dot_general(w_full, w_full, contract_rows, preferred_element_type=jnp.float32)
    blocks = w_full.reshape(-1, tile, rank_size)
    live = jnp.arange(slots, dtype=jnp.int32) < tile_count[0]
    picked = jnp.take(blocks, jnp.clip(tile_list, 0, blocks.shape[0] - 1), axis=0)
    picked = jnp.where(live[:, None, None], picked, jnp.zeros_like(picked))
    numerator = lax.dot_general(
        picked.reshape(slots * tile, rank_size),
        tiles.reshape(slots * tile, tiles.shape[2]),
        contract_rows,
        preferred_element_type=jnp.float32,
    )
    denominator = jnp.dot(
        gram, h_cols, precision=lax.Precision.HIGHEST, preferred_element_type=jnp.float32
    )
    return h_cols * numerator / denominator


def solution(mesh):
    placed = (
        P(("row", "col"), None, None),
        P(("row", "col")),
        P(("row", "col")),
        P(("row", "col"), None),
        P(None, ("row", "col")),
    )
    return jax.shard_map(
        shards, mesh=mesh, in_specs=placed, out_specs=P(None, ("row", "col")), check_vma=False
    )
```

```python
import jax
import jax.numpy as jnp
from jax import lax
from jax.sharding import PartitionSpec as P

contract_rows = (((0,), (0,)), ((), ()))
AXES = ("row", "col")


def doubling_order(n_row, n_col):
    col_bits = [1 << k for k in range(n_col.bit_length() - 1)][::-1]
    row_bits = [n_col << k for k in range(n_row.bit_length() - 1)][::-1]
    return col_bits + row_bits


def gather_rows(w_half, order, n):
    buf = w_half
    for mask in order:
        moved = lax.ppermute(buf, AXES, [(i, i ^ mask) for i in range(n)])
        buf = jnp.concatenate([buf, moved], axis=0)
    return buf


def slot_of(distance, order):
    pos = jnp.zeros_like(distance)
    for k, mask in enumerate(order):
        pos = pos + jnp.where((distance & mask) != 0, 1 << k, 0)
    return pos


def shards(tiles, tile_list, tile_count, w_rows, h_cols, n_row, n_col):
    slots, tile = tiles.shape[0], tiles.shape[1]
    rank_size = h_cols.shape[0]
    n = n_row * n_col
    share = w_rows.shape[0]
    w_half = w_rows.astype(jnp.bfloat16)
    order = doubling_order(n_row, n_col)
    buf = gather_rows(w_half, order, n)
    gram = lax.dot_general(buf, buf, contract_rows, preferred_element_type=jnp.float32)
    me = lax.axis_index("row") * n_col + lax.axis_index("col")
    per_block = tile // share
    blocks_total = n // per_block
    rows_of = jnp.clip(tile_list, 0, blocks_total - 1)
    owners = rows_of[:, None] * per_block + jnp.arange(per_block, dtype=jnp.int32)[None, :]
    where = slot_of(owners ^ me, order)
    pieces = buf.reshape(n, share, rank_size)
    picked = jnp.take(pieces, where.reshape(-1), axis=0).reshape(slots, tile, rank_size)
    live = jnp.arange(slots, dtype=jnp.int32) < tile_count[0]
    picked = jnp.where(live[:, None, None], picked, jnp.zeros_like(picked))
    numerator = lax.dot_general(
        picked.reshape(slots * tile, rank_size),
        tiles.reshape(slots * tile, tiles.shape[2]),
        contract_rows,
        preferred_element_type=jnp.float32,
    )
    denominator = jnp.dot(
        gram, h_cols, precision=lax.Precision.HIGHEST, preferred_element_type=jnp.float32
    )
    return h_cols * numerator / denominator


def solution(mesh):
    n_row, n_col = mesh.shape["row"], mesh.shape["col"]
    placed = (
        P(AXES, None, None),
        P(AXES),
        P(AXES),
        P(AXES, None),
        P(None, AXES),
    )

    def body(tiles, tile_list, tile_count, w_rows, h_cols):
        return shards(tiles, tile_list, tile_count, w_rows, h_cols, n_row, n_col)

    return jax.shard_map(
        body, mesh=mesh, in_specs=placed, out_specs=P(None, AXES), check_vma=False
    )
```

```python
import functools

import jax
import jax.numpy as jnp
from jax import lax
from jax.experimental import pallas as pl
from jax.experimental.pallas import tpu as pltpu
from jax.sharding import PartitionSpec as P

contract_rows = (((0,), (0,)), ((), ()))
AXES = ("row", "col")
COLUMN_CHUNK = 256


def doubling_order(n_row, n_col):
    col_bits = [1 << k for k in range(n_col.bit_length() - 1)][::-1]
    row_bits = [n_col << k for k in range(n_row.bit_length() - 1)][::-1]
    return col_bits + row_bits


def swap(value, mask, n):
    return lax.ppermute(value, AXES, [(i, i ^ mask) for i in range(n)])


def slot_of(distance, order):
    pos = jnp.zeros_like(distance)
    for k, mask in enumerate(order):
        pos = pos + jnp.where((distance & mask) != 0, 1 << k, 0)
    return pos


def slot_kernel(per_block, pos_ref, act_ref, acc_in, pieces_hbm, tiles_hbm, acc_out, w_vmem, t_vmem, sems):
    s = pl.program_id(0)
    tile = t_vmem.shape[0]

    @pl.when(s == 0)
    def _():
        acc_out[...] = acc_in[...]

    @pl.when(act_ref[s] != 0)
    def _():
        tile_copy = pltpu.make_async_copy(tiles_hbm.at[s], t_vmem, sems.at[per_block])
        tile_copy.start()
        for q in range(per_block):
            pltpu.make_async_copy(
                pieces_hbm.at[pos_ref[s * per_block + q]], w_vmem.at[q], sems.at[q]
            ).start()
        for q in range(per_block):
            pltpu.make_async_copy(pieces_hbm.at[0], w_vmem.at[q], sems.at[q]).wait()
        tile_copy.wait()
        w = w_vmem[...].reshape(tile, w_vmem.shape[2])
        for c in range(tile // COLUMN_CHUNK):
            cols = slice(c * COLUMN_CHUNK, (c + 1) * COLUMN_CHUNK)
            acc_out[:, cols] += lax.dot_general(
                w, t_vmem[:, cols], contract_rows, preferred_element_type=jnp.float32
            )


def slot_products(acc, pieces, tiles, pos, active):
    slots, tile, width = tiles.shape
    per_block, share, rank_size = pos.shape[1], pieces.shape[1], pieces.shape[2]
    kernel = functools.partial(slot_kernel, per_block)
    return pl.pallas_call(
        kernel,
        out_shape=jax.ShapeDtypeStruct(acc.shape, acc.dtype),
        grid_spec=pltpu.PrefetchScalarGridSpec(
            num_scalar_prefetch=2,
            grid=(slots,),
            in_specs=[
                pl.BlockSpec(acc.shape, lambda s, p, a: (0, 0)),
                pl.BlockSpec(memory_space=pl.ANY),
                pl.BlockSpec(memory_space=pl.ANY),
            ],
            out_specs=pl.BlockSpec(acc.shape, lambda s, p, a: (0, 0)),
            scratch_shapes=[
                pltpu.VMEM((per_block, share, rank_size), pieces.dtype),
                pltpu.VMEM((tile, width), tiles.dtype),
                pltpu.SemaphoreType.DMA((per_block + 1,)),
            ],
        ),
        input_output_aliases={2: 0},
        cost_estimate=pl.CostEstimate(
            flops=2 * slots * tile * width * rank_size,
            transcendentals=0,
            bytes_accessed=slots * (tile * width * 2 + tile * rank_size * 2) + 2 * acc.size * 4,
        ),
    )(pos.reshape(-1), active.astype(jnp.int32), acc, pieces, tiles)


def shards(tiles, tile_list, tile_count, w_rows, h_cols, n_row, n_col):
    slots, tile = tiles.shape[0], tiles.shape[1]
    rank_size = h_cols.shape[0]
    n = n_row * n_col
    share = w_rows.shape[0]
    order = doubling_order(n_row, n_col)
    steps = len(order)

    me = lax.axis_index("row") * n_col + lax.axis_index("col")
    per_block = tile // share
    blocks_total = n // per_block
    rows_of = jnp.clip(tile_list, 0, blocks_total - 1)
    owners = rows_of[:, None] * per_block + jnp.arange(per_block, dtype=jnp.int32)[None, :]
    where = slot_of(owners ^ me, order)
    need = functools.reduce(jnp.bitwise_or, [owners[:, q] ^ me for q in range(per_block)])
    done_at = jnp.full((slots,), -1, jnp.int32)
    for k, mask in enumerate(order):
        done_at = jnp.where((need & mask) != 0, k, done_at)
    live = jnp.arange(slots, dtype=jnp.int32) < tile_count[0]

    def phase(acc, source, base, first_step, last_step):
        active = live & (done_at >= first_step) & (done_at <= last_step)
        size = source.shape[0] // share
        pos = jnp.clip(where - base, 0, size - 1)
        return slot_products(acc, source.reshape(size, share, rank_size), tiles, pos, active)

    buf = w_rows.astype(jnp.bfloat16)
    gram = lax.dot_general(buf, buf, contract_rows, preferred_element_type=jnp.float32)
    for k in range(steps - 2):
        moved = swap(buf, order[k], n)
        gram = gram + lax.dot_general(moved, moved, contract_rows, preferred_element_type=jnp.float32)
        buf = jnp.concatenate([buf, moved], axis=0)

    zeros = jnp.zeros((rank_size, tiles.shape[2]), jnp.float32)
    moved = swap(buf, order[steps - 2], n)
    early = phase(zeros, buf, 0, -1, steps - 3)
    gram = gram + lax.dot_general(moved, moved, contract_rows, preferred_element_type=jnp.float32)
    moved, early = lax.optimization_barrier((moved, early))
    numerator = phase(zeros, moved, buf.shape[0] // share, steps - 2, steps - 2)
    buf = jnp.concatenate([buf, moved], axis=0)

    moved, partner_gram = swap((buf, gram), order[steps - 1], n)
    numerator = phase(numerator, moved, buf.shape[0] // share, steps - 1, steps - 1)
    gram = gram + partner_gram
    numerator = numerator + early

    denominator = jnp.dot(
        gram, h_cols, precision=lax.Precision.HIGHEST, preferred_element_type=jnp.float32
    )
    return h_cols * numerator / denominator


def solution(mesh):
    n_row, n_col = mesh.shape["row"], mesh.shape["col"]
    placed = (
        P(AXES, None, None),
        P(AXES),
        P(AXES),
        P(AXES, None),
        P(None, AXES),
    )

    def body(tiles, tile_list, tile_count, w_rows, h_cols):
        return shards(tiles, tile_list, tile_count, w_rows, h_cols, n_row, n_col)

    return jax.shard_map(
        body, mesh=mesh, in_specs=placed, out_specs=P(None, AXES), check_vma=False
    )
```

```python
import functools

import jax
import jax.numpy as jnp
from jax import lax
from jax.experimental import pallas as pl
from jax.experimental.pallas import tpu as pltpu
from jax.sharding import PartitionSpec as P

contract_rows = (((0,), (0,)), ((), ()))
AXES = ("row", "col")
COLUMN_CHUNK = 256


def doubling_order(n_row, n_col):
    col_bits = [1 << k for k in range(n_col.bit_length() - 1)][::-1]
    row_bits = [n_col << k for k in range(n_row.bit_length() - 1)][::-1]
    return col_bits + row_bits


def swap(value, mask, n):
    return lax.ppermute(value, AXES, [(i, i ^ mask) for i in range(n)])


def slot_of(distance, order):
    pos = jnp.zeros_like(distance)
    for k, mask in enumerate(order):
        pos = pos + jnp.where((distance & mask) != 0, 1 << k, 0)
    return pos


def slot_kernel(per_block, fresh, order_ref, count_ref, pos_ref, *refs):
    if fresh:
        pieces_hbm, tile_ref, acc_out, w_vmem, sems = refs
    else:
        acc_in, pieces_hbm, tile_ref, acc_out, w_vmem, sems = refs
    s = pl.program_id(0)
    tile = tile_ref.shape[1]

    @pl.when(s == 0)
    def _():
        if fresh:
            acc_out[...] = jnp.zeros(acc_out.shape, acc_out.dtype)
        else:
            acc_out[...] = acc_in[...]

    @pl.when(s < count_ref[0])
    def _():
        slot = order_ref[s]
        for q in range(per_block):
            pltpu.make_async_copy(
                pieces_hbm.at[pos_ref[slot * per_block + q]], w_vmem.at[q], sems.at[q]
            ).start()
        for q in range(per_block):
            pltpu.make_async_copy(pieces_hbm.at[0], w_vmem.at[q], sems.at[q]).wait()
        w_t = w_vmem[...].reshape(tile, w_vmem.shape[2]).T
        for c in range(tile_ref.shape[2] // COLUMN_CHUNK):
            cols = slice(c * COLUMN_CHUNK, (c + 1) * COLUMN_CHUNK)
            acc_out[:, cols] += jnp.dot(w_t, tile_ref[0, :, cols], preferred_element_type=jnp.float32)


def slot_products(acc, pieces, tiles, pos, active, rank_size):
    slots, tile, width = tiles.shape
    per_block, share = pos.shape[1], pieces.shape[1]
    count = jnp.sum(active.astype(jnp.int32))
    ranked = jnp.argsort(jnp.logical_not(active).astype(jnp.int32), stable=True).astype(jnp.int32)
    order = ranked[jnp.minimum(jnp.arange(slots, dtype=jnp.int32), jnp.maximum(count - 1, 0))]
    fresh = acc is None
    out_shape = jax.ShapeDtypeStruct((rank_size, width), jnp.float32)
    whole = pl.BlockSpec((rank_size, width), lambda s, o, c, p: (0, 0))
    in_specs = [
        pl.BlockSpec(memory_space=pl.ANY),
        pl.BlockSpec((1, tile, width), lambda s, o, c, p: (o[s], 0, 0)),
    ]
    operands = [pieces, tiles]
    if not fresh:
        in_specs = [whole] + in_specs
        operands = [acc] + operands
    return pl.pallas_call(
        functools.partial(slot_kernel, per_block, fresh),
        out_shape=out_shape,
        grid_spec=pltpu.PrefetchScalarGridSpec(
            num_scalar_prefetch=3,
            grid=(slots,),
            in_specs=in_specs,
            out_specs=whole,
            scratch_shapes=[
                pltpu.VMEM((per_block, share, rank_size), pieces.dtype),
                pltpu.SemaphoreType.DMA((per_block,)),
            ],
        ),
        input_output_aliases={} if fresh else {3: 0},
        cost_estimate=pl.CostEstimate(
            flops=2 * slots * tile * width * rank_size,
            transcendentals=0,
            bytes_accessed=slots * (tile * width * 2 + tile * rank_size * 2) + 2 * rank_size * width * 4,
        ),
    )(order, count.reshape(1), pos.reshape(-1), *operands)


def shards(tiles, tile_list, tile_count, w_rows, h_cols, n_row, n_col):
    slots, tile = tiles.shape[0], tiles.shape[1]
    rank_size = h_cols.shape[0]
    n = n_row * n_col
    share = w_rows.shape[0]
    order = doubling_order(n_row, n_col)
    steps = len(order)

    me = lax.axis_index("row") * n_col + lax.axis_index("col")
    per_block = tile // share
    blocks_total = n // per_block
    rows_of = jnp.clip(tile_list, 0, blocks_total - 1)
    owners = rows_of[:, None] * per_block + jnp.arange(per_block, dtype=jnp.int32)[None, :]
    where = slot_of(owners ^ me, order)
    need = functools.reduce(jnp.bitwise_or, [owners[:, q] ^ me for q in range(per_block)])
    done_at = jnp.full((slots,), -1, jnp.int32)
    for k, mask in enumerate(order):
        done_at = jnp.where((need & mask) != 0, k, done_at)
    live = jnp.arange(slots, dtype=jnp.int32) < tile_count[0]

    def phase(acc, source, base, first_step, last_step):
        active = live & (done_at >= first_step) & (done_at <= last_step)
        size = source.shape[0] // share
        pos = jnp.clip(where - base, 0, size - 1)
        return slot_products(acc, source.reshape(size, share, rank_size), tiles, pos, active, rank_size)

    buf = w_rows.astype(jnp.bfloat16)
    gram = lax.dot_general(buf, buf, contract_rows, preferred_element_type=jnp.float32)
    for k in range(steps - 2):
        moved = swap(buf, order[k], n)
        gram = gram + lax.dot_general(moved, moved, contract_rows, preferred_element_type=jnp.float32)
        buf = jnp.concatenate([buf, moved], axis=0)

    moved = swap(buf, order[steps - 2], n)
    early = phase(None, buf, 0, -1, steps - 3)
    gram = gram + lax.dot_general(moved, moved, contract_rows, preferred_element_type=jnp.float32)
    moved, early = lax.optimization_barrier((moved, early))
    numerator = phase(None, moved, buf.shape[0] // share, steps - 2, steps - 2)
    buf = jnp.concatenate([buf, moved], axis=0)

    moved, partner_gram = swap((buf, gram), order[steps - 1], n)
    numerator = phase(numerator, moved, buf.shape[0] // share, steps - 1, steps - 1)
    gram = gram + partner_gram
    numerator = numerator + early

    denominator = jnp.dot(
        gram, h_cols, precision=lax.Precision.HIGHEST, preferred_element_type=jnp.float32
    )
    return h_cols * numerator / denominator


def solution(mesh):
    n_row, n_col = mesh.shape["row"], mesh.shape["col"]
    placed = (
        P(AXES, None, None),
        P(AXES),
        P(AXES),
        P(AXES, None),
        P(None, AXES),
    )

    def body(tiles, tile_list, tile_count, w_rows, h_cols):
        return shards(tiles, tile_list, tile_count, w_rows, h_cols, n_row, n_col)

    return jax.shard_map(
        body, mesh=mesh, in_specs=placed, out_specs=P(None, AXES), check_vma=False
    )
```

```python
import jax
import jax.numpy as jnp
from jax import lax
from jax.sharding import Mesh
from jax.sharding import PartitionSpec as P

contract_rows = (((0,), (0,)), ((), ()))
SUB = ("rh", "core", "ch", "cl")


def swap(value, mask, n):
    return lax.ppermute(value, SUB, [(i, i ^ mask) for i in range(n)])


def gather_rows(w_half, n, n_col, col_masks):
    buf = w_half
    for mask in col_masks:
        buf = jnp.concatenate([buf, swap(buf, mask, n)], axis=0)
    group = lax.psum(1, ("rh", "cl"))
    spread = jnp.broadcast_to(buf[None], (group,) + buf.shape)
    buf = lax.all_to_all(spread, ("rh", "cl"), 0, 0, tiled=False).reshape(-1, buf.shape[1])
    return jnp.concatenate([buf, swap(buf, n_col, n)], axis=0)


def position_of(j, me, n_col, col_masks, group):
    near = jnp.zeros_like(j)
    for k, mask in enumerate(col_masks):
        near = near + jnp.where(((j ^ me) & mask) != 0, 1 << k, 0)
    first = 1 << len(col_masks)
    row_idx, col_idx = j // n_col, j % n_col
    member = (row_idx // 2) * 2 + (col_idx % 2)
    other_core = (row_idx % 2) != ((me // n_col) % 2)
    return jnp.where(other_core, group * first, 0) + member * first + near


def shards(tiles, tile_list, tile_count, w_rows, h_cols, n_row, n_col):
    slots, tile = tiles.shape[0], tiles.shape[1]
    rank_size = h_cols.shape[0]
    n = n_row * n_col
    share = w_rows.shape[0]
    col_masks = [2 << b for b in range(n_col.bit_length() - 2)][::-1]
    w_half = w_rows.astype(jnp.bfloat16)
    buf = gather_rows(w_half, n, n_col, col_masks)
    gram = lax.dot_general(buf, buf, contract_rows, preferred_element_type=jnp.float32)
    me = lax.axis_index(SUB)
    per_block = tile // share
    blocks_total = n // per_block
    rows_of = jnp.clip(tile_list, 0, blocks_total - 1)
    owners = rows_of[:, None] * per_block + jnp.arange(per_block, dtype=jnp.int32)[None, :]
    where = position_of(owners, me, n_col, col_masks, 2 * (n_row // 2))
    pieces = buf.reshape(n, share, rank_size)
    picked = jnp.take(pieces, where.reshape(-1), axis=0).reshape(slots, tile, rank_size)
    live = jnp.arange(slots, dtype=jnp.int32) < tile_count[0]
    picked = jnp.where(live[:, None, None], picked, jnp.zeros_like(picked))
    numerator = lax.dot_general(
        picked.reshape(slots * tile, rank_size),
        tiles.reshape(slots * tile, tiles.shape[2]),
        contract_rows,
        preferred_element_type=jnp.float32,
    )
    denominator = jnp.dot(
        gram, h_cols, precision=lax.Precision.HIGHEST, preferred_element_type=jnp.float32
    )
    return h_cols * numerator / denominator


def solution(mesh):
    n_row, n_col = mesh.shape["row"], mesh.shape["col"]
    sub = Mesh(mesh.devices.reshape(n_row // 2, 2, n_col // 2, 2), SUB)
    placed = (
        P(SUB, None, None),
        P(SUB),
        P(SUB),
        P(SUB, None),
        P(None, SUB),
    )

    def body(tiles, tile_list, tile_count, w_rows, h_cols):
        return shards(tiles, tile_list, tile_count, w_rows, h_cols, n_row, n_col)

    return jax.shard_map(
        body, mesh=sub, in_specs=placed, out_specs=P(None, SUB), check_vma=False
    )
```

```python
import jax
import jax.numpy as jnp
from jax import lax
from jax.sharding import Mesh
from jax.sharding import PartitionSpec as P

contract_rows = (((0,), (0,)), ((), ()))
SUB = ("rh", "core", "ch", "cl")


def swap(value, mask, n):
    return lax.ppermute(value, SUB, [(i, i ^ mask) for i in range(n)])


def gather_rows(w_half, n, n_col, col_masks):
    buf = w_half
    for mask in col_masks:
        buf = jnp.concatenate([buf, swap(buf, mask, n)], axis=0)
    group = lax.psum(1, ("rh", "cl"))
    spread = jnp.broadcast_to(buf[None], (group,) + buf.shape)
    buf = lax.all_to_all(spread, ("rh", "cl"), 0, 0, tiled=False).reshape(-1, buf.shape[1])
    pair = jnp.broadcast_to(buf[None], (2,) + buf.shape)
    return lax.all_to_all(pair, "core", 0, 0, tiled=False).reshape(-1, buf.shape[1])


def position_of(j, me, n_col, col_masks, group):
    near = jnp.zeros_like(j)
    for k, mask in enumerate(col_masks):
        near = near + jnp.where(((j ^ me) & mask) != 0, 1 << k, 0)
    first = 1 << len(col_masks)
    row_idx, col_idx = j // n_col, j % n_col
    member = (row_idx // 2) * 2 + (col_idx % 2)
    return (row_idx % 2) * (group * first) + member * first + near


def shards(tiles, tile_list, tile_count, w_rows, h_cols, n_row, n_col):
    slots, tile = tiles.shape[0], tiles.shape[1]
    rank_size = h_cols.shape[0]
    n = n_row * n_col
    share = w_rows.shape[0]
    col_masks = [2 << b for b in range(n_col.bit_length() - 2)][::-1]
    w_half = w_rows.astype(jnp.bfloat16)
    buf = gather_rows(w_half, n, n_col, col_masks)
    gram = lax.dot_general(buf, buf, contract_rows, preferred_element_type=jnp.float32)
    me = lax.axis_index(SUB)
    per_block = tile // share
    blocks_total = n // per_block
    rows_of = jnp.clip(tile_list, 0, blocks_total - 1)
    owners = rows_of[:, None] * per_block + jnp.arange(per_block, dtype=jnp.int32)[None, :]
    where = position_of(owners, me, n_col, col_masks, 2 * (n_row // 2))
    pieces = buf.reshape(n, share, rank_size)
    picked = jnp.take(pieces, where.reshape(-1), axis=0).reshape(slots, tile, rank_size)
    live = jnp.arange(slots, dtype=jnp.int32) < tile_count[0]
    picked = jnp.where(live[:, None, None], picked, jnp.zeros_like(picked))
    numerator = lax.dot_general(
        picked.reshape(slots * tile, rank_size),
        tiles.reshape(slots * tile, tiles.shape[2]),
        contract_rows,
        preferred_element_type=jnp.float32,
    )
    denominator = jnp.dot(
        gram, h_cols, precision=lax.Precision.HIGHEST, preferred_element_type=jnp.float32
    )
    return h_cols * numerator / denominator


def solution(mesh):
    n_row, n_col = mesh.shape["row"], mesh.shape["col"]
    sub = Mesh(mesh.devices.reshape(n_row // 2, 2, n_col // 2, 2), SUB)
    placed = (
        P(SUB, None, None),
        P(SUB),
        P(SUB),
        P(SUB, None),
        P(None, SUB),
    )

    def body(tiles, tile_list, tile_count, w_rows, h_cols):
        return shards(tiles, tile_list, tile_count, w_rows, h_cols, n_row, n_col)

    return jax.shard_map(
        body, mesh=sub, in_specs=placed, out_specs=P(None, SUB), check_vma=False
    )
```

```python
import jax
import jax.numpy as jnp
from jax import lax
from jax.sharding import Mesh
from jax.sharding import PartitionSpec as P

contract_rows = (((0,), (0,)), ((), ()))
SUB = ("rh", "core", "ch", "cl")


def swap(value, mask, n):
    return lax.ppermute(value, SUB, [(i, i ^ mask) for i in range(n)])


def gather_rows(w_half, n, n_col, col_masks):
    buf = w_half
    for mask in col_masks:
        buf = jnp.concatenate([buf, swap(buf, mask, n)], axis=0)
    group = lax.psum(1, ("rh", "cl"))
    spread = jnp.broadcast_to(buf[None], (group,) + buf.shape)
    buf = lax.all_to_all(spread, ("rh", "cl"), 0, 0, tiled=False).reshape(-1, buf.shape[1])
    return buf, swap(buf, n_col, n)


def position_of(j, me, n_col, col_masks, group):
    near = jnp.zeros_like(j)
    for k, mask in enumerate(col_masks):
        near = near + jnp.where(((j ^ me) & mask) != 0, 1 << k, 0)
    first = 1 << len(col_masks)
    row_idx, col_idx = j // n_col, j % n_col
    member = (row_idx // 2) * 2 + (col_idx % 2)
    other_core = (row_idx % 2) != ((me // n_col) % 2)
    return jnp.where(other_core, group * first, 0) + member * first + near


def shards(tiles, tile_list, tile_count, w_rows, h_cols, n_row, n_col):
    slots, tile = tiles.shape[0], tiles.shape[1]
    rank_size = h_cols.shape[0]
    n = n_row * n_col
    share = w_rows.shape[0]
    col_masks = [2 << b for b in range(n_col.bit_length() - 2)][::-1]
    w_half = w_rows.astype(jnp.bfloat16)
    mine, theirs = gather_rows(w_half, n, n_col, col_masks)
    gram = lax.dot_general(mine, mine, contract_rows, preferred_element_type=jnp.float32)
    gram = gram + lax.dot_general(theirs, theirs, contract_rows, preferred_element_type=jnp.float32)
    me = lax.axis_index(SUB)
    per_block = tile // share
    blocks_total = n // per_block
    rows_of = jnp.clip(tile_list, 0, blocks_total - 1)
    owners = rows_of[:, None] * per_block + jnp.arange(per_block, dtype=jnp.int32)[None, :]
    where = position_of(owners, me, n_col, col_masks, 2 * (n_row // 2))
    half = n // 2
    where = where.reshape(-1)
    near = jnp.take(mine.reshape(half, share, rank_size), where % half, axis=0)
    far = jnp.take(theirs.reshape(half, share, rank_size), where % half, axis=0)
    picked = jnp.where((where >= half)[:, None, None], far, near).reshape(slots, tile, rank_size)
    live = jnp.arange(slots, dtype=jnp.int32) < tile_count[0]
    picked = jnp.where(live[:, None, None], picked, jnp.zeros_like(picked))
    numerator = lax.dot_general(
        picked.reshape(slots * tile, rank_size),
        tiles.reshape(slots * tile, tiles.shape[2]),
        contract_rows,
        preferred_element_type=jnp.float32,
    )
    denominator = jnp.dot(
        gram, h_cols, precision=lax.Precision.HIGHEST, preferred_element_type=jnp.float32
    )
    return h_cols * numerator / denominator


def solution(mesh):
    n_row, n_col = mesh.shape["row"], mesh.shape["col"]
    sub = Mesh(mesh.devices.reshape(n_row // 2, 2, n_col // 2, 2), SUB)
    placed = (
        P(SUB, None, None),
        P(SUB),
        P(SUB),
        P(SUB, None),
        P(None, SUB),
    )

    def body(tiles, tile_list, tile_count, w_rows, h_cols):
        return shards(tiles, tile_list, tile_count, w_rows, h_cols, n_row, n_col)

    return jax.shard_map(
        body, mesh=sub, in_specs=placed, out_specs=P(None, SUB), check_vma=False
    )
```

```python
import jax
import jax.numpy as jnp
from jax import lax
from jax.sharding import Mesh
from jax.sharding import PartitionSpec as P

contract_rows = (((0,), (0,)), ((), ()))
SUB = ("rh", "core", "ch", "cl")


def swap(value, mask, n):
    return lax.ppermute(value, SUB, [(i, i ^ mask) for i in range(n)])


def gather_rows(w_half, me, n, n_col, col_masks):
    buf = w_half[None]
    for mask in col_masks:
        moved = swap(buf, mask, n)
        upper = (me & mask) != 0
        pair = jnp.where(upper, jnp.stack([moved, buf], axis=1), jnp.stack([buf, moved], axis=1))
        buf = pair.reshape((-1,) + w_half.shape)
    group = lax.psum(1, ("rh", "cl"))
    spread = jnp.broadcast_to(buf[None], (group,) + buf.shape)
    mine = lax.all_to_all(spread, ("rh", "cl"), 0, 1, tiled=False)
    mine = mine.reshape((buf.shape[0], group // 2, 2) + w_half.shape)
    return mine, swap(mine, n_col, n)


def shards(tiles, tile_list, tile_count, w_rows, h_cols, n_row, n_col):
    slots, tile = tiles.shape[0], tiles.shape[1]
    rank_size = h_cols.shape[0]
    n = n_row * n_col
    share = w_rows.shape[0]
    col_masks = [2 << b for b in range(n_col.bit_length() - 2)][::-1]
    me = lax.axis_index(SUB)
    w_half = w_rows.astype(jnp.bfloat16)
    mine, theirs = gather_rows(w_half, me, n, n_col, col_masks)
    flat_mine = mine.reshape(-1, rank_size)
    flat_theirs = theirs.reshape(-1, rank_size)
    gram = lax.dot_general(flat_mine, flat_mine, contract_rows, preferred_element_type=jnp.float32)
    gram = gram + lax.dot_general(flat_theirs, flat_theirs, contract_rows, preferred_element_type=jnp.float32)

    per_block = tile // share
    blocks_total = n // per_block
    first = jnp.clip(tile_list, 0, blocks_total - 1) * per_block
    row_idx, col_idx = first // n_col, first % n_col
    same_core = (row_idx % 2) == ((me // n_col) % 2)
    live = jnp.arange(slots, dtype=jnp.int32) < tile_count[0]
    picked = []
    for s in range(slots):
        start = (col_idx[s] // 2, row_idx[s] // 2, 0, 0, 0)
        size = (per_block // 2, 1, 2, share, rank_size)
        near = lax.dynamic_slice(mine, start, size)
        far = lax.dynamic_slice(theirs, start, size)
        block = jnp.where(same_core[s], near, far).reshape(tile, rank_size)
        picked.append(jnp.where(live[s], block, jnp.zeros_like(block)))
    picked = jnp.stack(picked)
    numerator = lax.dot_general(
        picked.reshape(slots * tile, rank_size),
        tiles.reshape(slots * tile, tiles.shape[2]),
        contract_rows,
        preferred_element_type=jnp.float32,
    )
    denominator = jnp.dot(
        gram, h_cols, precision=lax.Precision.HIGHEST, preferred_element_type=jnp.float32
    )
    return h_cols * numerator / denominator


def solution(mesh):
    n_row, n_col = mesh.shape["row"], mesh.shape["col"]
    sub = Mesh(mesh.devices.reshape(n_row // 2, 2, n_col // 2, 2), SUB)
    placed = (
        P(SUB, None, None),
        P(SUB),
        P(SUB),
        P(SUB, None),
        P(None, SUB),
    )

    def body(tiles, tile_list, tile_count, w_rows, h_cols):
        return shards(tiles, tile_list, tile_count, w_rows, h_cols, n_row, n_col)

    return jax.shard_map(
        body, mesh=sub, in_specs=placed, out_specs=P(None, SUB), check_vma=False
    )
```

```python
import jax
import jax.numpy as jnp
from jax import lax
from jax.sharding import Mesh
from jax.sharding import PartitionSpec as P

contract_rows = (((0,), (0,)), ((), ()))
SUB = ("rh", "core", "chh", "chl", "cl")
GROUP = ("rh", "chl", "cl")


def swap(value, mask, n):
    return lax.ppermute(value, SUB, [(i, i ^ mask) for i in range(n)])


def gather_rows(w_half, n, n_col, col_masks):
    buf = w_half
    for mask in col_masks:
        buf = jnp.concatenate([buf, swap(buf, mask, n)], axis=0)
    group = lax.psum(1, GROUP)
    spread = jnp.broadcast_to(buf[None], (group,) + buf.shape)
    buf = lax.all_to_all(spread, GROUP, 0, 0, tiled=False).reshape(-1, buf.shape[1])
    return buf, swap(buf, n_col, n)


def position_of(j, me, n_col, col_masks, group):
    near = jnp.zeros_like(j)
    for k, mask in enumerate(col_masks):
        near = near + jnp.where(((j ^ me) & mask) != 0, 1 << k, 0)
    first = 1 << len(col_masks)
    row_idx, col_idx = j // n_col, j % n_col
    member = (row_idx // 2) * 4 + col_idx % 4
    other_core = (row_idx % 2) != ((me // n_col) % 2)
    return jnp.where(other_core, group * first, 0) + member * first + near


def shards(tiles, tile_list, tile_count, w_rows, h_cols, n_row, n_col):
    slots, tile = tiles.shape[0], tiles.shape[1]
    rank_size = h_cols.shape[0]
    n = n_row * n_col
    share = w_rows.shape[0]
    col_masks = [4 << b for b in range(n_col.bit_length() - 3)][::-1]
    w_half = w_rows.astype(jnp.bfloat16)
    mine, theirs = gather_rows(w_half, n, n_col, col_masks)
    gram = lax.dot_general(mine, mine, contract_rows, preferred_element_type=jnp.float32)
    gram = gram + lax.dot_general(theirs, theirs, contract_rows, preferred_element_type=jnp.float32)
    me = lax.axis_index(SUB)
    per_block = tile // share
    blocks_total = n // per_block
    rows_of = jnp.clip(tile_list, 0, blocks_total - 1)
    owners = rows_of[:, None] * per_block + jnp.arange(per_block, dtype=jnp.int32)[None, :]
    where = position_of(owners, me, n_col, col_masks, 4 * (n_row // 2))
    half = n // 2
    where = where.reshape(-1)
    near = jnp.take(mine.reshape(half, share, rank_size), where % half, axis=0)
    far = jnp.take(theirs.reshape(half, share, rank_size), where % half, axis=0)
    picked = jnp.where((where >= half)[:, None, None], far, near).reshape(slots, tile, rank_size)
    live = jnp.arange(slots, dtype=jnp.int32) < tile_count[0]
    picked = jnp.where(live[:, None, None], picked, jnp.zeros_like(picked))
    numerator = lax.dot_general(
        picked.reshape(slots * tile, rank_size),
        tiles.reshape(slots * tile, tiles.shape[2]),
        contract_rows,
        preferred_element_type=jnp.float32,
    )
    denominator = jnp.dot(
        gram, h_cols, precision=lax.Precision.HIGHEST, preferred_element_type=jnp.float32
    )
    return h_cols * numerator / denominator


def solution(mesh):
    n_row, n_col = mesh.shape["row"], mesh.shape["col"]
    sub = Mesh(mesh.devices.reshape(n_row // 2, 2, n_col // 4, 2, 2), SUB)
    placed = (
        P(SUB, None, None),
        P(SUB),
        P(SUB),
        P(SUB, None),
        P(None, SUB),
    )

    def body(tiles, tile_list, tile_count, w_rows, h_cols):
        return shards(tiles, tile_list, tile_count, w_rows, h_cols, n_row, n_col)

    return jax.shard_map(
        body, mesh=sub, in_specs=placed, out_specs=P(None, SUB), check_vma=False
    )
```

```python
import jax
import jax.numpy as jnp
from jax import lax
from jax.sharding import Mesh
from jax.sharding import PartitionSpec as P

contract_rows = (((0,), (0,)), ((), ()))
SUB = ("rh", "core", "chh", "chl", "cl")
GROUP = ("rh", "chl", "cl")


def swap(value, mask, n):
    return lax.ppermute(value, SUB, [(i, i ^ mask) for i in range(n)])


def gather_rows(w_half, n, n_col, col_masks):
    buf = w_half
    for mask in col_masks:
        buf = jnp.concatenate([buf, swap(buf, mask, n)], axis=0)
    group = lax.psum(1, GROUP)
    spread = jnp.broadcast_to(buf[None], (group,) + buf.shape)
    buf = lax.all_to_all(spread, GROUP, 0, 0, tiled=False).reshape(-1, buf.shape[1])
    return buf, swap(buf, n_col, n)


def position_of(j, me, n_col, col_masks, group):
    near = jnp.zeros_like(j)
    for k, mask in enumerate(col_masks):
        near = near + jnp.where(((j ^ me) & mask) != 0, 1 << k, 0)
    first = 1 << len(col_masks)
    row_idx, col_idx = j // n_col, j % n_col
    member = (row_idx // 2) * 4 + col_idx % 4
    other_core = (row_idx % 2) != ((me // n_col) % 2)
    return jnp.where(other_core, group * first, 0) + member * first + near


def shards(tiles, tile_list, tile_count, w_rows, h_cols, n_row, n_col):
    slots, tile = tiles.shape[0], tiles.shape[1]
    rank_size = h_cols.shape[0]
    n = n_row * n_col
    share = w_rows.shape[0]
    col_masks = [4 << b for b in range(n_col.bit_length() - 3)][::-1]
    w_half = w_rows.astype(jnp.bfloat16)
    mine, theirs = gather_rows(w_half, n, n_col, col_masks)
    gram = lax.dot_general(mine, mine, contract_rows, preferred_element_type=jnp.float32)
    gram = gram + swap(gram, n_col, n)
    me = lax.axis_index(SUB)
    per_block = tile // share
    blocks_total = n // per_block
    rows_of = jnp.clip(tile_list, 0, blocks_total - 1)
    owners = rows_of[:, None] * per_block + jnp.arange(per_block, dtype=jnp.int32)[None, :]
    where = position_of(owners, me, n_col, col_masks, 4 * (n_row // 2))
    half = n // 2
    where = where.reshape(-1)
    near = jnp.take(mine.reshape(half, share, rank_size), where % half, axis=0)
    far = jnp.take(theirs.reshape(half, share, rank_size), where % half, axis=0)
    picked = jnp.where((where >= half)[:, None, None], far, near).reshape(slots, tile, rank_size)
    live = jnp.arange(slots, dtype=jnp.int32) < tile_count[0]
    picked = jnp.where(live[:, None, None], picked, jnp.zeros_like(picked))
    numerator = lax.dot_general(
        picked.reshape(slots * tile, rank_size),
        tiles.reshape(slots * tile, tiles.shape[2]),
        contract_rows,
        preferred_element_type=jnp.float32,
    )
    denominator = jnp.dot(
        gram, h_cols, precision=lax.Precision.HIGHEST, preferred_element_type=jnp.float32
    )
    return h_cols * numerator / denominator


def solution(mesh):
    n_row, n_col = mesh.shape["row"], mesh.shape["col"]
    sub = Mesh(mesh.devices.reshape(n_row // 2, 2, n_col // 4, 2, 2), SUB)
    placed = (
        P(SUB, None, None),
        P(SUB),
        P(SUB),
        P(SUB, None),
        P(None, SUB),
    )

    def body(tiles, tile_list, tile_count, w_rows, h_cols):
        return shards(tiles, tile_list, tile_count, w_rows, h_cols, n_row, n_col)

    return jax.shard_map(
        body, mesh=sub, in_specs=placed, out_specs=P(None, SUB), check_vma=False
    )
```

```python
import jax
import jax.numpy as jnp
from jax import lax
from jax.experimental import pallas as pl
from jax.experimental.pallas import tpu as pltpu
from jax.sharding import Mesh
from jax.sharding import PartitionSpec as P

contract_rows = (((0,), (0,)), ((), ()))
SUB = ("rh", "core", "chh", "chl", "cl")
GROUP = ("rh", "chl", "cl")


def swap(value, mask, n):
    return lax.ppermute(value, SUB, [(i, i ^ mask) for i in range(n)])


def gather_rows(w_half, n, n_col, col_masks):
    buf = w_half
    for mask in col_masks:
        buf = jnp.concatenate([buf, swap(buf, mask, n)], axis=0)
    group = lax.psum(1, GROUP)
    spread = jnp.broadcast_to(buf[None], (group,) + buf.shape)
    buf = lax.all_to_all(spread, GROUP, 0, 0, tiled=False).reshape(-1, buf.shape[1])
    return buf, swap(buf, n_col, n)


def position_of(j, me, n_col, col_masks, group):
    near = jnp.zeros_like(j)
    for k, mask in enumerate(col_masks):
        near = near + jnp.where(((j ^ me) & mask) != 0, 1 << k, 0)
    first = 1 << len(col_masks)
    row_idx, col_idx = j // n_col, j % n_col
    member = (row_idx // 2) * 4 + col_idx % 4
    other_core = (row_idx % 2) != ((me // n_col) % 2)
    return jnp.where(other_core, group * first, 0) + member * first + near


def pick_kernel(src_ref, far_ref, live_ref, mine_hbm, theirs_hbm, out_ref, sems):
    for p in range(out_ref.shape[0]):
        @pl.when((live_ref[p] != 0) & (far_ref[p] != 0))
        def _():
            pltpu.make_async_copy(theirs_hbm.at[src_ref[p]], out_ref.at[p], sems.at[p]).start()

        @pl.when((live_ref[p] != 0) & (far_ref[p] == 0))
        def _():
            pltpu.make_async_copy(mine_hbm.at[src_ref[p]], out_ref.at[p], sems.at[p]).start()

        @pl.when(live_ref[p] == 0)
        def _():
            out_ref[p] = jnp.zeros(out_ref.shape[1:], out_ref.dtype)

    for p in range(out_ref.shape[0]):
        @pl.when(live_ref[p] != 0)
        def _():
            pltpu.make_async_copy(mine_hbm.at[0], out_ref.at[p], sems.at[p]).wait()


def pick_pieces(mine, theirs, src, far, live):
    count = src.shape[0]
    piece = mine.shape[1:]
    return pl.pallas_call(
        pick_kernel,
        out_shape=jax.ShapeDtypeStruct((count,) + piece, mine.dtype),
        grid_spec=pltpu.PrefetchScalarGridSpec(
            num_scalar_prefetch=3,
            grid=(),
            in_specs=[pl.BlockSpec(memory_space=pl.ANY), pl.BlockSpec(memory_space=pl.ANY)],
            out_specs=pl.BlockSpec((count,) + piece, lambda *_: (0, 0, 0)),
            scratch_shapes=[pltpu.SemaphoreType.DMA((count,))],
        ),
        cost_estimate=pl.CostEstimate(
            flops=0, transcendentals=0, bytes_accessed=2 * count * piece[0] * piece[1] * 2
        ),
    )(src, far, live, mine, theirs)


def shards(tiles, tile_list, tile_count, w_rows, h_cols, n_row, n_col):
    slots, tile = tiles.shape[0], tiles.shape[1]
    rank_size = h_cols.shape[0]
    n = n_row * n_col
    share = w_rows.shape[0]
    col_masks = [4 << b for b in range(n_col.bit_length() - 3)][::-1]
    w_half = w_rows.astype(jnp.bfloat16)
    mine, theirs = gather_rows(w_half, n, n_col, col_masks)
    gram = lax.dot_general(mine, mine, contract_rows, preferred_element_type=jnp.float32)
    gram = gram + lax.dot_general(theirs, theirs, contract_rows, preferred_element_type=jnp.float32)
    me = lax.axis_index(SUB)
    per_block = tile // share
    blocks_total = n // per_block
    rows_of = jnp.clip(tile_list, 0, blocks_total - 1)
    owners = rows_of[:, None] * per_block + jnp.arange(per_block, dtype=jnp.int32)[None, :]
    where = position_of(owners, me, n_col, col_masks, 4 * (n_row // 2))
    half = n // 2
    where = where.reshape(-1)
    live = jnp.arange(slots, dtype=jnp.int32) < tile_count[0]
    live_piece = jnp.repeat(live, per_block).astype(jnp.int32)
    picked = pick_pieces(
        mine.reshape(half, share, rank_size),
        theirs.reshape(half, share, rank_size),
        jnp.clip(where % half, 0, half - 1),
        (where >= half).astype(jnp.int32),
        live_piece,
    ).reshape(slots, tile, rank_size)
    numerator = lax.dot_general(
        picked.reshape(slots * tile, rank_size),
        tiles.reshape(slots * tile, tiles.shape[2]),
        contract_rows,
        preferred_element_type=jnp.float32,
    )
    denominator = jnp.dot(
        gram, h_cols, precision=lax.Precision.HIGHEST, preferred_element_type=jnp.float32
    )
    return h_cols * numerator / denominator


def solution(mesh):
    n_row, n_col = mesh.shape["row"], mesh.shape["col"]
    sub = Mesh(mesh.devices.reshape(n_row // 2, 2, n_col // 4, 2, 2), SUB)
    placed = (
        P(SUB, None, None),
        P(SUB),
        P(SUB),
        P(SUB, None),
        P(None, SUB),
    )

    def body(tiles, tile_list, tile_count, w_rows, h_cols):
        return shards(tiles, tile_list, tile_count, w_rows, h_cols, n_row, n_col)

    return jax.shard_map(
        body, mesh=sub, in_specs=placed, out_specs=P(None, SUB), check_vma=False
    )
```

```python
import jax
import jax.numpy as jnp
from jax import lax
from jax.sharding import Mesh
from jax.sharding import PartitionSpec as P

contract_rows = (((0,), (0,)), ((), ()))
SUB = ("rh", "core", "chh", "chl", "cl")
GROUP = ("rh", "chl", "cl")


def swap(value, mask, n):
    return lax.ppermute(value, SUB, [(i, i ^ mask) for i in range(n)])


def gather_rows(w_half, n, n_col, col_masks):
    buf = w_half
    for mask in col_masks:
        buf = jnp.concatenate([buf, swap(buf, mask, n)], axis=0)
    group = lax.psum(1, GROUP)
    spread = jnp.broadcast_to(buf[None], (group,) + buf.shape)
    return lax.all_to_all(spread, GROUP, 0, 0, tiled=False).reshape(-1, buf.shape[1])


def position_of(j, me, n_col, col_masks, group):
    near = jnp.zeros_like(j)
    for k, mask in enumerate(col_masks):
        near = near + jnp.where(((j ^ me) & mask) != 0, 1 << k, 0)
    first = 1 << len(col_masks)
    row_idx, col_idx = j // n_col, j % n_col
    member = (row_idx // 2) * 4 + col_idx % 4
    other_core = (row_idx % 2) != ((me // n_col) % 2)
    return jnp.where(other_core, group * first, 0) + member * first + near


def shards(tiles, tile_list, tile_count, w_rows, h_cols, n_row, n_col):
    slots, tile = tiles.shape[0], tiles.shape[1]
    rank_size = h_cols.shape[0]
    n = n_row * n_col
    share = w_rows.shape[0]
    col_masks = [4 << b for b in range(n_col.bit_length() - 3)][::-1]
    w_half = w_rows.astype(jnp.bfloat16)
    me = lax.axis_index(SUB)
    partner = me ^ n_col
    request = swap(jnp.concatenate([tile_list, tile_count]), n_col, n)
    mine = gather_rows(w_half, n, n_col, col_masks)
    half = n // 2
    pieces = mine.reshape(half, share, rank_size)
    per_block = tile // share
    blocks_total = n // per_block
    lanes = jnp.arange(per_block, dtype=jnp.int32)[None, :]

    def positions(blocks, device):
        owners = jnp.clip(blocks, 0, blocks_total - 1)[:, None] * per_block + lanes
        return position_of(owners, device, n_col, col_masks, 4 * (n_row // 2)).reshape(-1)

    where = positions(tile_list, me)
    for_partner = jnp.take(pieces, positions(request[:slots], partner) % half, axis=0)
    own_gram = lax.dot_general(mine, mine, contract_rows, preferred_element_type=jnp.float32)
    far = swap(for_partner, n_col, n)
    gram = own_gram + swap(own_gram, n_col, n)
    near = jnp.take(pieces, where % half, axis=0)
    picked = jnp.where((where >= half)[:, None, None], far, near).reshape(slots, tile, rank_size)
    live = jnp.arange(slots, dtype=jnp.int32) < tile_count[0]
    picked = jnp.where(live[:, None, None], picked, jnp.zeros_like(picked))
    numerator = lax.dot_general(
        picked.reshape(slots * tile, rank_size),
        tiles.reshape(slots * tile, tiles.shape[2]),
        contract_rows,
        preferred_element_type=jnp.float32,
    )
    denominator = jnp.dot(
        gram, h_cols, precision=lax.Precision.HIGHEST, preferred_element_type=jnp.float32
    )
    return h_cols * numerator / denominator


def solution(mesh):
    n_row, n_col = mesh.shape["row"], mesh.shape["col"]
    sub = Mesh(mesh.devices.reshape(n_row // 2, 2, n_col // 4, 2, 2), SUB)
    placed = (
        P(SUB, None, None),
        P(SUB),
        P(SUB),
        P(SUB, None),
        P(None, SUB),
    )

    def body(tiles, tile_list, tile_count, w_rows, h_cols):
        return shards(tiles, tile_list, tile_count, w_rows, h_cols, n_row, n_col)

    return jax.shard_map(
        body, mesh=sub, in_specs=placed, out_specs=P(None, SUB), check_vma=False
    )
```

```python
import jax
import jax.numpy as jnp
from jax import lax
from jax.sharding import Mesh
from jax.sharding import PartitionSpec as P

contract_rows = (((0,), (0,)), ((), ()))
SUB = ("rh", "core", "chh", "chl", "cl")
GROUP = ("rh", "chl", "cl")


def swap(value, mask, n):
    return lax.ppermute(value, SUB, [(i, i ^ mask) for i in range(n)])


def gather_rows(w_half, n, n_col, col_masks):
    buf = w_half
    for mask in col_masks:
        buf = jnp.concatenate([buf, swap(buf, mask, n)], axis=0)
    group = lax.psum(1, GROUP)
    spread = jnp.broadcast_to(buf[None], (group,) + buf.shape)
    buf = lax.all_to_all(spread, GROUP, 0, 0, tiled=False).reshape(-1, buf.shape[1])
    return buf, swap(buf, n_col, n)


def position_of(j, me, n_col, col_masks, group):
    near = jnp.zeros_like(j)
    for k, mask in enumerate(col_masks):
        near = near + jnp.where(((j ^ me) & mask) != 0, 1 << k, 0)
    first = 1 << len(col_masks)
    row_idx, col_idx = j // n_col, j % n_col
    member = (row_idx // 2) * 4 + col_idx % 4
    other_core = (row_idx % 2) != ((me // n_col) % 2)
    return jnp.where(other_core, group * first, 0) + member * first + near


def shards(tiles, tile_list, tile_count, w_rows, h_cols, n_row, n_col):
    slots, tile = tiles.shape[0], tiles.shape[1]
    rank_size = h_cols.shape[0]
    n = n_row * n_col
    share = w_rows.shape[0]
    col_masks = [4 << b for b in range(n_col.bit_length() - 3)][::-1]
    w_half = w_rows.astype(jnp.bfloat16)
    mine, theirs = gather_rows(w_half, n, n_col, col_masks)
    gram = lax.dot_general(mine, mine, contract_rows, preferred_element_type=jnp.float32)
    gram = gram + lax.dot_general(theirs, theirs, contract_rows, preferred_element_type=jnp.float32)
    me = lax.axis_index(SUB)
    per_block = tile // share
    blocks_total = n // per_block
    rows_of = jnp.clip(tile_list, 0, blocks_total - 1)
    owners = rows_of[:, None] * per_block + jnp.arange(per_block, dtype=jnp.int32)[None, :]
    where = position_of(owners, me, n_col, col_masks, 4 * (n_row // 2))
    half = n // 2
    where = where.reshape(-1)
    index = where % half
    near_src = mine.reshape(half, share, rank_size)
    far_src = theirs.reshape(half, share, rank_size)
    near = jnp.stack([lax.dynamic_index_in_dim(near_src, index[p], keepdims=False) for p in range(index.shape[0])])
    far = jnp.stack([lax.dynamic_index_in_dim(far_src, index[p], keepdims=False) for p in range(index.shape[0])])
    picked = jnp.where((where >= half)[:, None, None], far, near).reshape(slots, tile, rank_size)
    live = jnp.arange(slots, dtype=jnp.int32) < tile_count[0]
    picked = jnp.where(live[:, None, None], picked, jnp.zeros_like(picked))
    numerator = lax.dot_general(
        picked.reshape(slots * tile, rank_size),
        tiles.reshape(slots * tile, tiles.shape[2]),
        contract_rows,
        preferred_element_type=jnp.float32,
    )
    denominator = jnp.dot(
        gram, h_cols, precision=lax.Precision.HIGHEST, preferred_element_type=jnp.float32
    )
    return h_cols * numerator / denominator


def solution(mesh):
    n_row, n_col = mesh.shape["row"], mesh.shape["col"]
    sub = Mesh(mesh.devices.reshape(n_row // 2, 2, n_col // 4, 2, 2), SUB)
    placed = (
        P(SUB, None, None),
        P(SUB),
        P(SUB),
        P(SUB, None),
        P(None, SUB),
    )

    def body(tiles, tile_list, tile_count, w_rows, h_cols):
        return shards(tiles, tile_list, tile_count, w_rows, h_cols, n_row, n_col)

    return jax.shard_map(
        body, mesh=sub, in_specs=placed, out_specs=P(None, SUB), check_vma=False
    )
```

```python
import jax
import jax.numpy as jnp
from jax import lax
from jax.sharding import Mesh
from jax.sharding import PartitionSpec as P

contract_rows = (((0,), (0,)), ((), ()))
SUB = ("rh", "core", "chh", "chl", "cl")
GROUP = ("rh", "chl", "cl")


def swap(value, mask, n):
    return lax.ppermute(value, SUB, [(i, i ^ mask) for i in range(n)])


def gather_rows(w_half, n, n_col, col_masks):
    buf = w_half
    for mask in col_masks:
        buf = jnp.concatenate([buf, swap(buf, mask, n)], axis=0)
    group = lax.psum(1, GROUP)
    spread = jnp.broadcast_to(buf[None], (group,) + buf.shape)
    buf = lax.all_to_all(spread, GROUP, 0, 0, tiled=False).reshape(-1, buf.shape[1])
    return buf, swap(buf, n_col, n)


def position_of(j, me, n_col, col_masks, group):
    near = jnp.zeros_like(j)
    for k, mask in enumerate(col_masks):
        near = near + jnp.where(((j ^ me) & mask) != 0, 1 << k, 0)
    first = 1 << len(col_masks)
    row_idx, col_idx = j // n_col, j % n_col
    member = (row_idx // 2) * 4 + col_idx % 4
    other_core = (row_idx % 2) != ((me // n_col) % 2)
    return jnp.where(other_core, group * first, 0) + member * first + near


def shards(tiles, tile_list, tile_count, w_rows, h_cols, n_row, n_col):
    slots, tile = tiles.shape[0], tiles.shape[1]
    rank_size = h_cols.shape[0]
    n = n_row * n_col
    share = w_rows.shape[0]
    col_masks = [4 << b for b in range(n_col.bit_length() - 3)][::-1]
    w_half = w_rows.astype(jnp.bfloat16)
    mine, theirs = gather_rows(w_half, n, n_col, col_masks)
    gram = lax.dot_general(mine, mine, contract_rows, preferred_element_type=jnp.float32)
    gram = gram + lax.dot_general(theirs, theirs, contract_rows, preferred_element_type=jnp.float32)
    me = lax.axis_index(SUB)
    per_block = tile // share
    blocks_total = n // per_block
    rows_of = jnp.clip(tile_list, 0, blocks_total - 1)
    owners = rows_of[:, None] * per_block + jnp.arange(per_block, dtype=jnp.int32)[None, :]
    where = position_of(owners, me, n_col, col_masks, 4 * (n_row // 2))
    half = n // 2
    where = where.reshape(-1)
    index = where % half
    near = mine.reshape(half, share, rank_size).at[index].get(mode="promise_in_bounds")
    far = theirs.reshape(half, share, rank_size).at[index].get(mode="promise_in_bounds")
    picked = jnp.where((where >= half)[:, None, None], far, near).reshape(slots, tile, rank_size)
    live = jnp.arange(slots, dtype=jnp.int32) < tile_count[0]
    picked = jnp.where(live[:, None, None], picked, jnp.zeros_like(picked))
    numerator = lax.dot_general(
        picked.reshape(slots * tile, rank_size),
        tiles.reshape(slots * tile, tiles.shape[2]),
        contract_rows,
        preferred_element_type=jnp.float32,
    )
    denominator = jnp.dot(
        gram, h_cols, precision=lax.Precision.HIGHEST, preferred_element_type=jnp.float32
    )
    return h_cols * numerator / denominator


def solution(mesh):
    n_row, n_col = mesh.shape["row"], mesh.shape["col"]
    sub = Mesh(mesh.devices.reshape(n_row // 2, 2, n_col // 4, 2, 2), SUB)
    placed = (
        P(SUB, None, None),
        P(SUB),
        P(SUB),
        P(SUB, None),
        P(None, SUB),
    )

    def body(tiles, tile_list, tile_count, w_rows, h_cols):
        return shards(tiles, tile_list, tile_count, w_rows, h_cols, n_row, n_col)

    return jax.shard_map(
        body, mesh=sub, in_specs=placed, out_specs=P(None, SUB), check_vma=False
    )
```

```python
import jax
import jax.numpy as jnp
from jax import lax
from jax.sharding import Mesh
from jax.sharding import PartitionSpec as P

contract_rows = (((0,), (0,)), ((), ()))
SUB = ("rh", "core", "chh", "chl", "cl")
GROUP = ("rh", "chl", "cl")


def swap(value, mask, n):
    return lax.ppermute(value, SUB, [(i, i ^ mask) for i in range(n)])


def gather_rows(w_half, n, n_col, col_masks):
    buf = w_half
    for mask in col_masks:
        buf = jnp.concatenate([buf, swap(buf, mask, n)], axis=0)
    group = lax.psum(1, GROUP)
    spread = jnp.broadcast_to(buf[None], (group,) + buf.shape)
    buf = lax.all_to_all(spread, GROUP, 0, 0, tiled=False).reshape(-1, buf.shape[1])
    return buf, swap(buf, n_col, n)


def position_of(j, me, n_col, col_masks, group):
    near = jnp.zeros_like(j)
    for k, mask in enumerate(col_masks):
        near = near + jnp.where(((j ^ me) & mask) != 0, 1 << k, 0)
    first = 1 << len(col_masks)
    row_idx, col_idx = j // n_col, j % n_col
    member = (row_idx // 2) * 4 + col_idx % 4
    other_core = (row_idx % 2) != ((me // n_col) % 2)
    return jnp.where(other_core, group * first, 0) + member * first + near


def shards(tiles, tile_list, tile_count, w_rows, h_cols, n_row, n_col):
    slots, tile = tiles.shape[0], tiles.shape[1]
    rank_size = h_cols.shape[0]
    n = n_row * n_col
    share = w_rows.shape[0]
    col_masks = [4 << b for b in range(n_col.bit_length() - 3)][::-1]
    w_half = w_rows.astype(jnp.bfloat16)
    mine, theirs = gather_rows(w_half, n, n_col, col_masks)
    own_gram = lax.dot_general(mine, mine, contract_rows, preferred_element_type=jnp.float32)
    me = lax.axis_index(SUB)
    per_block = tile // share
    blocks_total = n // per_block
    rows_of = jnp.clip(tile_list, 0, blocks_total - 1)
    owners = rows_of[:, None] * per_block + jnp.arange(per_block, dtype=jnp.int32)[None, :]
    where = position_of(owners, me, n_col, col_masks, 4 * (n_row // 2))
    half = n // 2
    where = where.reshape(-1)
    near = jnp.take(mine.reshape(half, share, rank_size), where % half, axis=0)
    far = jnp.take(theirs.reshape(half, share, rank_size), where % half, axis=0)
    picked = jnp.where((where >= half)[:, None, None], far, near).reshape(slots, tile, rank_size)
    live = jnp.arange(slots, dtype=jnp.int32) < tile_count[0]
    picked = jnp.where(live[:, None, None], picked, jnp.zeros_like(picked))
    own_gram, picked = lax.optimization_barrier((own_gram, picked))
    gram = own_gram + swap(own_gram, n_col, n)
    numerator = lax.dot_general(
        picked.reshape(slots * tile, rank_size),
        tiles.reshape(slots * tile, tiles.shape[2]),
        contract_rows,
        preferred_element_type=jnp.float32,
    )
    denominator = jnp.dot(
        gram, h_cols, precision=lax.Precision.HIGHEST, preferred_element_type=jnp.float32
    )
    return h_cols * numerator / denominator


def solution(mesh):
    n_row, n_col = mesh.shape["row"], mesh.shape["col"]
    sub = Mesh(mesh.devices.reshape(n_row // 2, 2, n_col // 4, 2, 2), SUB)
    placed = (
        P(SUB, None, None),
        P(SUB),
        P(SUB),
        P(SUB, None),
        P(None, SUB),
    )

    def body(tiles, tile_list, tile_count, w_rows, h_cols):
        return shards(tiles, tile_list, tile_count, w_rows, h_cols, n_row, n_col)

    return jax.shard_map(
        body, mesh=sub, in_specs=placed, out_specs=P(None, SUB), check_vma=False
    )
```

```python
import jax
import jax.numpy as jnp
from jax import lax
from jax.sharding import Mesh
from jax.sharding import PartitionSpec as P

contract_rows = (((0,), (0,)), ((), ()))
SUB = ("rh", "core", "chh", "chl", "cl")
GROUP = ("rh", "chl", "cl")


def swap(value, mask, n):
    return lax.ppermute(value, SUB, [(i, i ^ mask) for i in range(n)])


def gather_rows(w_half, n, n_col, col_masks):
    buf = w_half
    for mask in col_masks:
        buf = jnp.concatenate([buf, swap(buf, mask, n)], axis=0)
    group = lax.psum(1, GROUP)
    spread = jnp.broadcast_to(buf[None], (group,) + buf.shape)
    buf = lax.all_to_all(spread, GROUP, 0, 0, tiled=False).reshape(-1, buf.shape[1])
    return buf, swap(buf, n_col, n)


def position_of(j, me, n_col, col_masks, group):
    near = jnp.zeros_like(j)
    for k, mask in enumerate(col_masks):
        near = near + jnp.where(((j ^ me) & mask) != 0, 1 << k, 0)
    first = 1 << len(col_masks)
    row_idx, col_idx = j // n_col, j % n_col
    member = (row_idx // 2) * 4 + col_idx % 4
    other_core = (row_idx % 2) != ((me // n_col) % 2)
    return jnp.where(other_core, group * first, 0) + member * first + near


def shards(tiles, tile_list, tile_count, w_rows, h_cols, n_row, n_col):
    slots, tile = tiles.shape[0], tiles.shape[1]
    rank_size = h_cols.shape[0]
    n = n_row * n_col
    share = w_rows.shape[0]
    col_masks = [4 << b for b in range(n_col.bit_length() - 3)][::-1]
    w_half = w_rows.astype(jnp.bfloat16)
    mine, theirs = gather_rows(w_half, n, n_col, col_masks)
    own_gram = lax.dot_general(mine, mine, contract_rows, preferred_element_type=jnp.float32)
    me = lax.axis_index(SUB)
    per_block = tile // share
    blocks_total = n // per_block
    rows_of = jnp.clip(tile_list, 0, blocks_total - 1)
    owners = rows_of[:, None] * per_block + jnp.arange(per_block, dtype=jnp.int32)[None, :]
    where = position_of(owners, me, n_col, col_masks, 4 * (n_row // 2))
    half = n // 2
    where = where.reshape(-1)
    near = jnp.take(mine.reshape(half, share, rank_size), where % half, axis=0)
    far = jnp.take(theirs.reshape(half, share, rank_size), where % half, axis=0)
    own_gram, far = lax.optimization_barrier((own_gram, far))
    gram = own_gram + swap(own_gram, n_col, n)
    picked = jnp.where((where >= half)[:, None, None], far, near).reshape(slots, tile, rank_size)
    live = jnp.arange(slots, dtype=jnp.int32) < tile_count[0]
    picked = jnp.where(live[:, None, None], picked, jnp.zeros_like(picked))
    gram, picked = lax.optimization_barrier((gram, picked))
    numerator = lax.dot_general(
        picked.reshape(slots * tile, rank_size),
        tiles.reshape(slots * tile, tiles.shape[2]),
        contract_rows,
        preferred_element_type=jnp.float32,
    )
    denominator = jnp.dot(
        gram, h_cols, precision=lax.Precision.HIGHEST, preferred_element_type=jnp.float32
    )
    return h_cols * numerator / denominator


def solution(mesh):
    n_row, n_col = mesh.shape["row"], mesh.shape["col"]
    sub = Mesh(mesh.devices.reshape(n_row // 2, 2, n_col // 4, 2, 2), SUB)
    placed = (
        P(SUB, None, None),
        P(SUB),
        P(SUB),
        P(SUB, None),
        P(None, SUB),
    )

    def body(tiles, tile_list, tile_count, w_rows, h_cols):
        return shards(tiles, tile_list, tile_count, w_rows, h_cols, n_row, n_col)

    return jax.shard_map(
        body, mesh=sub, in_specs=placed, out_specs=P(None, SUB), check_vma=False
    )
```
